128 devices in a mesh: owner: 32 (over z, x, core), tensor: 4 (over y).
Axes of the slice: x: 4, y: 4, z: 4, core: 2. Of those that a mesh axis runs over, the one named last changes fastest.
Arguments:
- gradients: bfloat16 [160, 1536, 512], P(None, 'owner', 'tensor'), may hold values from -12 to 12
- moments: bfloat16 [160, 1536, 512], P(None, 'owner', 'tensor'), may hold values from -12 to 12
- stats: float32 [256, 512, 512], P(('owner', 'tensor')), may hold values from -1 to 11, as said below
- bases: float32 [256, 512, 512], P(('owner', 'tensor')), may hold values from -1 to 2
- second: bfloat16 [256, 1536, 512], P(('owner', 'tensor')), may hold values from 0.19921875 to 8
- owner_list: int32 [160], replicated, may hold values from 0 to 127, as said below
Outputs:
- new_moments: bfloat16 [160, 1536, 512], P(None, 'owner', 'tensor')
- update: bfloat16 [160, 1536, 512], P(None, 'owner', 'tensor')
- new_stats: float32 [256, 512, 512], P(('owner', 'tensor'))
- new_bases: float32 [256, 512, 512], P(('owner', 'tensor'))
- new_second: bfloat16 [256, 1536, 512], P(('owner', 'tensor'))
The draws below stay inside these ranges and needn't reach their ends.
Inputs may be any that keep to these rules, and one draw needn't show every extreme that they name: `owner_list`: no device owns more than 2 matrices, and at least one owns 2. `stats`: Symmetric.
All inputs are finite; a program needn't handle non-finite values.
Results may differ from the reference program's by a relative error of at most 0.0077.
Values may be sent and summed in bfloat16 or wider, within the bound.
No kernel may reach another device: no remote copies, remote signals or barrier semaphores. Data moves between devices by JAX's collectives and lax.ppermute only.
A program may use at most 128 MiB of HBM per device.

```python
import math
import jax
import jax.numpy as jnp
from jax import lax

ROWS = 1536
COLS = 512
CAP = 2
NM = 160
SLOTS = 256
N_OWNER = 32
N_TENSOR = 4


def draw_owner_list(key, part):
    devices = N_OWNER * N_TENSOR
    chosen = jax.random.permutation(key, devices * CAP)[:NM]
    return (chosen // CAP).astype(jnp.int32)


def draw_stats(key, part):
    total = N_OWNER * N_TENSOR * CAP
    key_noise = jax.random.fold_in(key, 11)
    key_diag = jax.random.fold_in(key, 12)
    noise = jax.random.truncated_normal(key_noise, -4.0, 4.0, (total, COLS, COLS), jnp.float32)
    symmetric = (noise + jnp.swapaxes(noise, 1, 2)) * (0.45 / (1.4142135 * COLS ** 0.5))
    diag_vals = jax.random.uniform(key_diag, (total, COLS), jnp.float32, 1.0, 3.0)
    eye_mat = jnp.eye(COLS, dtype=jnp.float32)
    return symmetric + diag_vals[:, :, None] * eye_mat[None, :, :]


def draw_bases(key, part):
    total = N_OWNER * N_TENSOR * CAP
    key_noise = jax.random.fold_in(key, 21)
    noise = jax.random.truncated_normal(key_noise, -4.0, 4.0, (total, COLS, COLS), jnp.float32)
    eye_mat = jnp.eye(COLS, dtype=jnp.float32)
    return eye_mat[None, :, :] + noise * (0.3 / COLS ** 0.5)


def block_scale(own_key, shape, cuts, smallest, largest):
    def one(dim, blocks):
        heights = jax.random.uniform(jax.random.fold_in(jax.random.fold_in(own_key, 6), dim), (blocks,), jnp.float32, smallest / len(cuts), largest / len(cuts))
        return jnp.repeat(jnp.exp(heights), shape[dim] // blocks).reshape((-1,) + (1,) * (len(shape) - dim - 1))

    loudness = one(*cuts[0])
    for cut in cuts[1:]:
        loudness = loudness * one(*cut)
    return loudness


def centred(key, extent, deviation, most, shards=(), kind=jnp.bfloat16):
    entries = jax.random.normal(key, extent, jnp.float32) * deviation
    if len(shards) > 0:
        entries = block_scale(key, extent, shards, -0.22, 0.18) * entries
    return jnp.clip(entries, min=-most, max=most).astype(kind)


def setup_inputs(seed: int = 0) -> dict:
    key_list = jax.random.split(jax.random.key(seed), 7)
    return {
        "gradients": centred(key_list[0], (NM, ROWS, COLS), 2.0, 12.0, ((1, 32), (2, 4))),
        "moments": centred(key_list[1], (NM, ROWS, COLS), 2.0, 12.0, ((1, 32), (2, 4))),
        "stats": draw_stats(jax.random.fold_in(key_list[6], 71), 0),
        "bases": draw_bases(jax.random.fold_in(key_list[6], 71), 0),
        "second": jnp.clip(jnp.exp(math.log(8.0) - 3.6927934 * jax.random.uniform(key_list[4], (SLOTS, ROWS, COLS), jnp.float32) ** block_scale(key_list[4], (SLOTS, ROWS, COLS), ((0, 128),), -0.2, 0.2)), 0.19921875, 8.0).astype(jnp.bfloat16),
        "owner_list": draw_owner_list(jax.random.fold_in(key_list[6], 71), 0),
    }


def refine(iterate):
    for sweep in range(2):
        iter_b = iterate.astype(jnp.bfloat16)
        square = jnp.dot(iter_b.T, iter_b, preferred_element_type=jnp.float32).astype(jnp.bfloat16)
        iterate = 1.5 * iterate - 0.5 * jnp.dot(iter_b, square, preferred_element_type=jnp.float32)
    return iterate

def reference(gradients, moments, stats, bases, second, owner_list):
    slot_total = N_OWNER * N_TENSOR * CAP
    matrix_ids = jnp.arange(NM, dtype=jnp.int32)
    shared = owner_list[:, None] == owner_list[None, :]
    earlier = matrix_ids[:, None] < matrix_ids[None, :]
    position = lax.optimization_barrier(jnp.sum((shared & earlier).astype(jnp.int32), axis=0))
    slot_id = (owner_list * CAP + position).astype(jnp.int32)
    new_moments = (0.9 * moments.astype(jnp.float32) + 0.1 * gradients.astype(jnp.float32)).astype(jnp.bfloat16)

    def one_matrix(which):
        slot_now = slot_id[which]
        grad_mat = gradients[which]
        moment_mat = new_moments[which]
        stat_old = stats[slot_now]
        basis_old = bases[slot_now]
        second_old = second[slot_now].astype(jnp.float32)
        gram = jnp.dot(grad_mat.T, grad_mat, preferred_element_type=jnp.float32)
        stat_next = 0.95 * stat_old + 0.05 / ROWS * gram
        basis_b = basis_old.astype(jnp.bfloat16)
        rotated = jnp.dot(grad_mat, basis_b, preferred_element_type=jnp.float32)
        second_next = 0.95 * second_old + 0.05 * rotated * rotated
        moment_rot = jnp.dot(moment_mat, basis_b, preferred_element_type=jnp.float32)
        scaled = (moment_rot / (jnp.sqrt(second_next) + 1e-06)).astype(jnp.bfloat16)
        step_mat = jnp.dot(scaled, basis_b.T, preferred_element_type=jnp.float32).astype(jnp.bfloat16)
        power = jnp.dot(stat_next, basis_old, precision=lax.Precision.HIGHEST, preferred_element_type=jnp.float32)
        iterate = power / (2.0 * jnp.sqrt(COLS * jnp.mean(power * power) + 1e-06))
        return (step_mat, stat_next, refine(iterate), second_next.astype(jnp.bfloat16))
    steps_all, stats_all, bases_all, second_all = lax.map(one_matrix, matrix_ids)
    new_stats = jnp.zeros((slot_total, COLS, COLS), jnp.float32).at[slot_id].set(stats_all)
    new_bases = jnp.zeros((slot_total, COLS, COLS), jnp.float32).at[slot_id].set(bases_all)
    new_second = jnp.zeros((slot_total, ROWS, COLS), jnp.bfloat16).at[slot_id].set(second_all)
    return (new_moments, steps_all, new_stats, new_bases, new_second)
```

```python
import jax
import jax.numpy as jnp
from jax import lax
from jax.sharding import PartitionSpec as P


def refine(iterate):
    for sweep in range(2):
        iter_b = iterate.astype(jnp.bfloat16)
        square = jnp.einsum(
            "cki,ckj->cij", iter_b, iter_b, preferred_element_type=jnp.float32
        ).astype(jnp.bfloat16)
        iterate = 1.5 * iterate - 0.5 * jnp.einsum(
            "cik,ckj->cij", iter_b, square, preferred_element_type=jnp.float32
        )
    return iterate


def exchange(pieces):
    return lax.all_to_all(
        pieces, ("owner", "tensor"), split_axis=1, concat_axis=1, tiled=True
    )


def local(gradients, moments, stats, bases, second, owner_list):
    matrices, piece_rows, piece_cols = gradients.shape
    capacity = stats.shape[0]
    owners = lax.axis_size("owner")
    tensors = lax.axis_size("tensor")
    devices = owners * tensors
    myself = lax.axis_index(("owner", "tensor"))
    matrix_ids = jnp.arange(matrices, dtype=jnp.int32)
    shared = owner_list[:, None] == owner_list[None, :]
    earlier = matrix_ids[:, None] < matrix_ids[None, :]
    position = jnp.sum((shared & earlier).astype(jnp.int32), axis=0)
    slot_id = owner_list * capacity + position
    targets = (
        jnp.arange(devices, dtype=jnp.int32)[None, :] * capacity
        + jnp.arange(capacity, dtype=jnp.int32)[:, None]
    )
    hit = targets[:, :, None] == slot_id[None, None, :]
    which = jnp.sum(jnp.where(hit, matrix_ids[None, None, :], 0), axis=2)

    send_grads = jnp.take(gradients, which, axis=0, mode="clip")
    got_grads = exchange(send_grads)

    new_moments = (0.9 * moments.astype(jnp.float32) + 0.1 * gradients.astype(jnp.float32)).astype(
        jnp.bfloat16
    )
    send_moms = jnp.take(new_moments, which, axis=0, mode="clip")
    got_moms = exchange(send_moms)

    def assemble(pieces):
        blocks = pieces.reshape(capacity, owners, tensors, piece_rows, piece_cols)
        return blocks.transpose(0, 1, 3, 2, 4).reshape(
            capacity, owners * piece_rows, tensors * piece_cols
        )

    grad_mats = assemble(got_grads)
    full_rows = grad_mats.shape[1]
    full_cols = grad_mats.shape[2]
    gram = jnp.einsum("cri,crj->cij", grad_mats, grad_mats, preferred_element_type=jnp.float32)
    stat_next = 0.95 * stats + 0.05 / full_rows * gram
    basis_b = bases.astype(jnp.bfloat16)
    rotated = jnp.einsum("crk,ckj->crj", grad_mats, basis_b, preferred_element_type=jnp.float32)
    second_next = 0.95 * second.astype(jnp.float32) + 0.05 * rotated * rotated
    power = jnp.einsum(
        "cij,cjk->cik",
        stat_next,
        bases,
        precision=lax.Precision.HIGHEST,
        preferred_element_type=jnp.float32,
    )
    iterate = power / (
        2.0 * jnp.sqrt(full_cols * jnp.mean(power * power, axis=(1, 2), keepdims=True) + 1e-06)
    )
    iterate = refine(iterate)

    moment_mats = assemble(got_moms)
    moment_rot = jnp.einsum(
        "crk,ckj->crj", moment_mats, basis_b, preferred_element_type=jnp.float32
    )
    scaled = (moment_rot / (jnp.sqrt(second_next) + 1e-06)).astype(jnp.bfloat16)
    step_mats = jnp.einsum(
        "crj,ckj->crk", scaled, basis_b, preferred_element_type=jnp.float32
    ).astype(jnp.bfloat16)
    step_pieces = step_mats.reshape(capacity, owners, piece_rows, tensors, piece_cols).transpose(
        0, 1, 3, 2, 4
    )
    returned = exchange(step_pieces.reshape(capacity, devices, piece_rows, piece_cols))
    back_index = position * devices + owner_list
    update = jnp.take(
        returned.reshape(capacity * devices, piece_rows, piece_cols), back_index, axis=0,
        mode="clip",
    )

    my_slots = myself * capacity + jnp.arange(capacity, dtype=jnp.int32)
    filled = jnp.any(my_slots[:, None] == slot_id[None, :], axis=1)[:, None, None]
    new_stats = jnp.where(filled, stat_next, 0.0)
    new_bases = jnp.where(filled, iterate, 0.0)
    new_second = jnp.where(filled, second_next, 0.0).astype(jnp.bfloat16)
    return (new_moments, update, new_stats, new_bases, new_second)


def solution(mesh):
    placed = (
        P(None, "owner", "tensor"),
        P(None, "owner", "tensor"),
        P(("owner", "tensor"), None, None),
        P(("owner", "tensor"), None, None),
        P(("owner", "tensor"), None, None),
        P(),
    )
    return jax.shard_map(
        local,
        mesh=mesh,
        in_specs=placed,
        out_specs=(
            P(None, "owner", "tensor"),
            P(None, "owner", "tensor"),
            P(("owner", "tensor"), None, None),
            P(("owner", "tensor"), None, None),
            P(("owner", "tensor"), None, None),
        ),
        check_vma=False,
    )
```

```python
import jax
import jax.numpy as jnp
from jax import lax
from jax.sharding import PartitionSpec as P


def refine(iterate):
    for sweep in range(2):
        iter_b = iterate.astype(jnp.bfloat16)
        square = jnp.einsum(
            "cki,ckj->cij", iter_b, iter_b, preferred_element_type=jnp.float32
        ).astype(jnp.bfloat16)
        iterate = 1.5 * iterate - 0.5 * jnp.einsum(
            "cik,ckj->cij", iter_b, square, preferred_element_type=jnp.float32
        )
    return iterate


def exchange(pieces):
    return lax.all_to_all(
        pieces, ("tensor", "owner"), split_axis=0, concat_axis=0, tiled=True
    )


def local(gradients, moments, stats, bases, second, owner_list):
    matrices, piece_rows, piece_cols = gradients.shape
    capacity = stats.shape[0]
    owners = lax.axis_size("owner")
    tensors = lax.axis_size("tensor")
    devices = owners * tensors
    myself = lax.axis_index(("owner", "tensor"))
    matrix_ids = jnp.arange(matrices, dtype=jnp.int32)
    shared = owner_list[:, None] == owner_list[None, :]
    earlier = matrix_ids[:, None] < matrix_ids[None, :]
    position = jnp.sum((shared & earlier).astype(jnp.int32), axis=0)
    slot_id = owner_list * capacity + position
    place = jnp.arange(devices, dtype=jnp.int32)
    device_at = (place % owners) * tensors + place // owners
    targets = device_at[:, None] * capacity + jnp.arange(capacity, dtype=jnp.int32)[None, :]
    hit = targets[:, :, None] == slot_id[None, None, :]
    which = jnp.sum(jnp.where(hit, matrix_ids[None, None, :], 0), axis=2)

    got_grads = [exchange(jnp.take(gradients, which[:, c], axis=0, mode="clip")) for c in range(capacity)]
    new_moments = (0.9 * moments.astype(jnp.float32) + 0.1 * gradients.astype(jnp.float32)).astype(
        jnp.bfloat16
    )
    got_moms = [exchange(jnp.take(new_moments, which[:, c], axis=0, mode="clip")) for c in range(capacity)]

    def column_blocks(pieces):
        return pieces.reshape(tensors, owners * piece_rows, piece_cols)

    full_rows = owners * piece_rows
    full_cols = tensors * piece_cols
    basis_b = bases.astype(jnp.bfloat16)
    returned, stat_list, second_list = [], [], []
    for c in range(capacity):
        grad_b = column_blocks(got_grads[c])
        basis_rows = basis_b[c].reshape(tensors, piece_cols, full_cols)
        gram = jnp.einsum(
            "tik,sil->tksl", grad_b, grad_b, preferred_element_type=jnp.float32
        ).reshape(full_cols, full_cols)
        stat_list.append(0.95 * stats[c] + 0.05 / full_rows * gram)
        rotated = jnp.einsum(
            "tik,tkj->ij", grad_b, basis_rows, preferred_element_type=jnp.float32
        )
        second_next = 0.95 * second[c].astype(jnp.float32) + 0.05 * rotated * rotated
        second_list.append(second_next)
        moment_rot = jnp.einsum(
            "tik,tkj->ij", column_blocks(got_moms[c]), basis_rows,
            preferred_element_type=jnp.float32,
        )
        scaled = (moment_rot / (jnp.sqrt(second_next) + 1e-06)).astype(jnp.bfloat16)
        step_b = jnp.einsum(
            "ij,tkj->tik", scaled, basis_rows, preferred_element_type=jnp.float32
        ).astype(jnp.bfloat16)
        returned.append(exchange(step_b.reshape(devices, piece_rows, piece_cols)))
    owner_place = (owner_list % tensors) * owners + owner_list // tensors
    update = jnp.take(
        jnp.concatenate(returned, axis=0), position * devices + owner_place, axis=0, mode="clip"
    )

    stat_next = jnp.stack(stat_list)
    second_next = jnp.stack(second_list)
    power = jnp.einsum(
        "cij,cjk->cik",
        stat_next,
        bases,
        precision=lax.Precision.HIGHEST,
        preferred_element_type=jnp.float32,
    )
    iterate = power / (
        2.0 * jnp.sqrt(full_cols * jnp.mean(power * power, axis=(1, 2), keepdims=True) + 1e-06)
    )
    iterate = refine(iterate)

    my_slots = myself * capacity + jnp.arange(capacity, dtype=jnp.int32)
    filled = jnp.any(my_slots[:, None] == slot_id[None, :], axis=1)[:, None, None]
    new_stats = jnp.where(filled, stat_next, 0.0)
    new_bases = jnp.where(filled, iterate, 0.0)
    new_second = jnp.where(filled, second_next, 0.0).astype(jnp.bfloat16)
    return (new_moments, update, new_stats, new_bases, new_second)


def solution(mesh):
    placed = (
        P(None, "owner", "tensor"),
        P(None, "owner", "tensor"),
        P(("owner", "tensor"), None, None),
        P(("owner", "tensor"), None, None),
        P(("owner", "tensor"), None, None),
        P(),
    )
    return jax.shard_map(
        local,
        mesh=mesh,
        in_specs=placed,
        out_specs=(
            P(None, "owner", "tensor"),
            P(None, "owner", "tensor"),
            P(("owner", "tensor"), None, None),
            P(("owner", "tensor"), None, None),
            P(("owner", "tensor"), None, None),
        ),
        check_vma=False,
    )
```

```python
import jax
import jax.numpy as jnp
from jax import lax
from jax.sharding import PartitionSpec as P


def refine(iterate):
    for sweep in range(2):
        iter_b = iterate.astype(jnp.bfloat16)
        square = jnp.einsum(
            "cki,ckj->cij", iter_b, iter_b, preferred_element_type=jnp.float32
        ).astype(jnp.bfloat16)
        iterate = 1.5 * iterate - 0.5 * jnp.einsum(
            "cik,ckj->cij", iter_b, square, preferred_element_type=jnp.float32
        )
    return iterate


def exchange(pieces):
    return lax.all_to_all(
        pieces, ("tensor", "owner"), split_axis=0, concat_axis=0, tiled=True
    )


def local(gradients, moments, stats, bases, second, owner_list):
    matrices, piece_rows, piece_cols = gradients.shape
    capacity = stats.shape[0]
    owners = lax.axis_size("owner")
    tensors = lax.axis_size("tensor")
    devices = owners * tensors
    myself = lax.axis_index(("owner", "tensor"))
    matrix_ids = jnp.arange(matrices, dtype=jnp.int32)
    shared = owner_list[:, None] == owner_list[None, :]
    earlier = matrix_ids[:, None] < matrix_ids[None, :]
    position = jnp.sum((shared & earlier).astype(jnp.int32), axis=0)
    slot_id = owner_list * capacity + position
    place = jnp.arange(devices, dtype=jnp.int32)
    device_at = (place % owners) * tensors + place // owners
    targets = device_at[:, None] * capacity + jnp.arange(capacity, dtype=jnp.int32)[None, :]
    hit = targets[:, :, None] == slot_id[None, None, :]
    which = jnp.sum(jnp.where(hit, matrix_ids[None, None, :], 0), axis=2)

    new_moments = (0.9 * moments.astype(jnp.float32) + 0.1 * gradients.astype(jnp.float32)).astype(
        jnp.bfloat16
    )
    outgoing = jnp.stack(
        [jnp.take(gradients, which, axis=0, mode="clip"), jnp.take(new_moments, which, axis=0, mode="clip")],
        axis=2,
    )
    incoming = exchange(outgoing)

    def column_blocks(pieces):
        return pieces.reshape(tensors, owners * piece_rows, piece_cols)

    full_rows = owners * piece_rows
    full_cols = tensors * piece_cols
    basis_b = bases.astype(jnp.bfloat16)
    steps, stat_list, second_list = [], [], []
    for c in range(capacity):
        grad_b = column_blocks(incoming[:, c, 0])
        basis_rows = basis_b[c].reshape(tensors, piece_cols, full_cols)
        gram = jnp.einsum(
            "tik,sil->tksl", grad_b, grad_b, preferred_element_type=jnp.float32
        ).reshape(full_cols, full_cols)
        stat_list.append(0.95 * stats[c] + 0.05 / full_rows * gram)
        rotated = jnp.einsum(
            "tik,tkj->ij", grad_b, basis_rows, preferred_element_type=jnp.float32
        )
        second_next = 0.95 * second[c].astype(jnp.float32) + 0.05 * rotated * rotated
        second_list.append(second_next)
        moment_rot = jnp.einsum(
            "tik,tkj->ij", column_blocks(incoming[:, c, 1]), basis_rows,
            preferred_element_type=jnp.float32,
        )
        scaled = (moment_rot / (jnp.sqrt(second_next) + 1e-06)).astype(jnp.bfloat16)
        step_b = jnp.einsum(
            "ij,tkj->tik", scaled, basis_rows, preferred_element_type=jnp.float32
        ).astype(jnp.bfloat16)
        steps.append(step_b.reshape(devices, piece_rows, piece_cols))
    returned = exchange(jnp.stack(steps, axis=1))
    owner_place = (owner_list % tensors) * owners + owner_list // tensors
    update = jnp.take(
        returned.reshape(devices * capacity, piece_rows, piece_cols),
        owner_place * capacity + position, axis=0, mode="clip",
    )

    stat_next = jnp.stack(stat_list)
    second_next = jnp.stack(second_list)
    power = jnp.einsum(
        "cij,cjk->cik",
        stat_next,
        bases,
        precision=lax.Precision.HIGHEST,
        preferred_element_type=jnp.float32,
    )
    iterate = power / (
        2.0 * jnp.sqrt(full_cols * jnp.mean(power * power, axis=(1, 2), keepdims=True) + 1e-06)
    )
    iterate = refine(iterate)

    my_slots = myself * capacity + jnp.arange(capacity, dtype=jnp.int32)
    filled = jnp.any(my_slots[:, None] == slot_id[None, :], axis=1)[:, None, None]
    new_stats = jnp.where(filled, stat_next, 0.0)
    new_bases = jnp.where(filled, iterate, 0.0)
    new_second = jnp.where(filled, second_next, 0.0).astype(jnp.bfloat16)
    return (new_moments, update, new_stats, new_bases, new_second)


def solution(mesh):
    placed = (
        P(None, "owner", "tensor"),
        P(None, "owner", "tensor"),
        P(("owner", "tensor"), None, None),
        P(("owner", "tensor"), None, None),
        P(("owner", "tensor"), None, None),
        P(),
    )
    return jax.shard_map(
        local,
        mesh=mesh,
        in_specs=placed,
        out_specs=(
            P(None, "owner", "tensor"),
            P(None, "owner", "tensor"),
            P(("owner", "tensor"), None, None),
            P(("owner", "tensor"), None, None),
            P(("owner", "tensor"), None, None),
        ),
        check_vma=False,
    )
```

```python
import jax
import jax.numpy as jnp
from jax import lax
from jax.sharding import PartitionSpec as P


def refine(iterate):
    for sweep in range(2):
        iter_b = iterate.astype(jnp.bfloat16)
        square = jnp.einsum(
            "cki,ckj->cij", iter_b, iter_b, preferred_element_type=jnp.float32
        ).astype(jnp.bfloat16)
        iterate = 1.5 * iterate - 0.5 * jnp.einsum(
            "cik,ckj->cij", iter_b, square, preferred_element_type=jnp.float32
        )
    return iterate


def exchange(pieces):
    return lax.all_to_all(
        pieces, ("tensor", "owner"), split_axis=0, concat_axis=0, tiled=True
    )


def local(gradients, moments, stats, bases, second, owner_list):
    matrices, piece_rows, piece_cols = gradients.shape
    capacity = stats.shape[0]
    owners = lax.axis_size("owner")
    tensors = lax.axis_size("tensor")
    devices = owners * tensors
    myself = lax.axis_index(("owner", "tensor"))
    matrix_ids = jnp.arange(matrices, dtype=jnp.int32)
    shared = owner_list[:, None] == owner_list[None, :]
    earlier = matrix_ids[:, None] < matrix_ids[None, :]
    position = jnp.sum((shared & earlier).astype(jnp.int32), axis=0)
    slot_id = owner_list * capacity + position
    place = jnp.arange(devices, dtype=jnp.int32)
    device_at = (place % owners) * tensors + place // owners
    targets = device_at[:, None] * capacity + jnp.arange(capacity, dtype=jnp.int32)[None, :]
    hit = targets[:, :, None] == slot_id[None, None, :]
    which = jnp.sum(jnp.where(hit, matrix_ids[None, None, :], 0), axis=2)

    got_grads = exchange(jnp.take(gradients, which, axis=0, mode="clip"))
    new_moments = (0.9 * moments.astype(jnp.float32) + 0.1 * gradients.astype(jnp.float32)).astype(
        jnp.bfloat16
    )
    got_moms = exchange(jnp.take(new_moments, which, axis=0, mode="clip"))

    def column_blocks(pieces):
        return pieces.reshape(tensors, owners * piece_rows, piece_cols)

    full_rows = owners * piece_rows
    full_cols = tensors * piece_cols
    basis_b = bases.astype(jnp.bfloat16)
    stat_list, second_list = [], []
    for c in range(capacity):
        grad_b = column_blocks(got_grads[:, c])
        basis_rows = basis_b[c].reshape(tensors, piece_cols, full_cols)
        gram = jnp.einsum(
            "tik,sil->tksl", grad_b, grad_b, preferred_element_type=jnp.float32
        ).reshape(full_cols, full_cols)
        stat_list.append(0.95 * stats[c] + 0.05 / full_rows * gram)
        rotated = jnp.einsum(
            "tik,tkj->ij", grad_b, basis_rows, preferred_element_type=jnp.float32
        )
        second_list.append(0.95 * second[c].astype(jnp.float32) + 0.05 * rotated * rotated)
    got_moms, second_list = lax.optimization_barrier((got_moms, second_list))
    steps = []
    for c in range(capacity):
        basis_rows = basis_b[c].reshape(tensors, piece_cols, full_cols)
        moment_rot = jnp.einsum(
            "tik,tkj->ij", column_blocks(got_moms[:, c]), basis_rows,
            preferred_element_type=jnp.float32,
        )
        scaled = (moment_rot / (jnp.sqrt(second_list[c]) + 1e-06)).astype(jnp.bfloat16)
        step_b = jnp.einsum(
            "ij,tkj->tik", scaled, basis_rows, preferred_element_type=jnp.float32
        ).astype(jnp.bfloat16)
        steps.append(step_b.reshape(devices, piece_rows, piece_cols))
    returned = exchange(jnp.stack(steps, axis=1))
    owner_place = (owner_list % tensors) * owners + owner_list // tensors
    update = jnp.take(
        returned.reshape(devices * capacity, piece_rows, piece_cols),
        owner_place * capacity + position, axis=0, mode="clip",
    )

    stat_next = jnp.stack(stat_list)
    second_next = jnp.stack(second_list)
    power = jnp.einsum(
        "cij,cjk->cik",
        stat_next,
        bases,
        precision=lax.Precision.HIGHEST,
        preferred_element_type=jnp.float32,
    )
    iterate = power / (
        2.0 * jnp.sqrt(full_cols * jnp.mean(power * power, axis=(1, 2), keepdims=True) + 1e-06)
    )
    iterate = refine(iterate)

    my_slots = myself * capacity + jnp.arange(capacity, dtype=jnp.int32)
    filled = jnp.any(my_slots[:, None] == slot_id[None, :], axis=1)[:, None, None]
    new_stats = jnp.where(filled, stat_next, 0.0)
    new_bases = jnp.where(filled, iterate, 0.0)
    new_second = jnp.where(filled, second_next, 0.0).astype(jnp.bfloat16)
    return (new_moments, update, new_stats, new_bases, new_second)


def solution(mesh):
    placed = (
        P(None, "owner", "tensor"),
        P(None, "owner", "tensor"),
        P(("owner", "tensor"), None, None),
        P(("owner", "tensor"), None, None),
        P(("owner", "tensor"), None, None),
        P(),
    )
    return jax.shard_map(
        local,
        mesh=mesh,
        in_specs=placed,
        out_specs=(
            P(None, "owner", "tensor"),
            P(None, "owner", "tensor"),
            P(("owner", "tensor"), None, None),
            P(("owner", "tensor"), None, None),
            P(("owner", "tensor"), None, None),
        ),
        check_vma=False,
    )
```

```python
import jax
import jax.numpy as jnp
from jax import lax
from jax.sharding import PartitionSpec as P


def refine(iterate):
    for sweep in range(2):
        iter_b = iterate.astype(jnp.bfloat16)
        square = jnp.einsum(
            "cki,ckj->cij", iter_b, iter_b, preferred_element_type=jnp.float32
        ).astype(jnp.bfloat16)
        iterate = 1.5 * iterate - 0.5 * jnp.einsum(
            "cik,ckj->cij", iter_b, square, preferred_element_type=jnp.float32
        )
    return iterate


def exchange(pieces):
    return lax.all_to_all(
        pieces, ("tensor", "owner"), split_axis=0, concat_axis=0, tiled=True
    )


def local(gradients, moments, stats, bases, second, owner_list):
    matrices, piece_rows, piece_cols = gradients.shape
    capacity = stats.shape[0]
    owners = lax.axis_size("owner")
    tensors = lax.axis_size("tensor")
    devices = owners * tensors
    myself = lax.axis_index(("owner", "tensor"))
    matrix_ids = jnp.arange(matrices, dtype=jnp.int32)
    shared = owner_list[:, None] == owner_list[None, :]
    earlier = matrix_ids[:, None] < matrix_ids[None, :]
    position = jnp.sum((shared & earlier).astype(jnp.int32), axis=0)
    slot_id = owner_list * capacity + position
    place = jnp.arange(devices, dtype=jnp.int32)
    device_at = (place % owners) * tensors + place // owners
    targets = device_at[:, None] * capacity + jnp.arange(capacity, dtype=jnp.int32)[None, :]
    hit = targets[:, :, None] == slot_id[None, None, :]
    which = jnp.sum(jnp.where(hit, matrix_ids[None, None, :], 0), axis=2)

    got_grads = exchange(jnp.take(gradients, which, axis=0, mode="clip"))
    new_moments = (0.9 * moments.astype(jnp.float32) + 0.1 * gradients.astype(jnp.float32)).astype(
        jnp.bfloat16
    )
    got_moms = exchange(jnp.take(new_moments, which, axis=0, mode="clip"))

    def column_blocks(pieces):
        return pieces.reshape(tensors, owners * piece_rows, piece_cols)

    full_rows = owners * piece_rows
    full_cols = tensors * piece_cols
    basis_b = bases.astype(jnp.bfloat16)
    stat_list, second_list = [], []
    for c in range(capacity):
        grad_b = column_blocks(got_grads[:, c])
        basis_rows = basis_b[c].reshape(tensors, piece_cols, full_cols)
        gram = jnp.einsum(
            "tik,sil->tksl", grad_b, grad_b, preferred_element_type=jnp.float32
        ).reshape(full_cols, full_cols)
        stat_list.append(0.95 * stats[c] + 0.05 / full_rows * gram)
        rotated = jnp.einsum(
            "tik,tkj->ij", grad_b, basis_rows, preferred_element_type=jnp.float32
        )
        second_list.append(0.95 * second[c].astype(jnp.float32) + 0.05 * rotated * rotated)
    got_moms, second_list = lax.optimization_barrier((got_moms, second_list))
    steps = []
    for c in range(capacity):
        basis_rows = basis_b[c].reshape(tensors, piece_cols, full_cols)
        moment_rot = jnp.einsum(
            "tik,tkj->ij", column_blocks(got_moms[:, c]), basis_rows,
            preferred_element_type=jnp.float32,
        )
        scaled = (moment_rot / (jnp.sqrt(second_list[c]) + 1e-06)).astype(jnp.bfloat16)
        scaled = lax.optimization_barrier(scaled)
        step_b = jnp.einsum(
            "ij,tkj->tik", scaled, basis_rows, preferred_element_type=jnp.float32
        ).astype(jnp.bfloat16)
        steps.append(step_b.reshape(devices, piece_rows, piece_cols))
    returned = exchange(jnp.stack(steps, axis=1))
    owner_place = (owner_list % tensors) * owners + owner_list // tensors
    update = jnp.take(
        returned.reshape(devices * capacity, piece_rows, piece_cols),
        owner_place * capacity + position, axis=0, mode="clip",
    )

    stat_next = jnp.stack(stat_list)
    second_next = jnp.stack(second_list)
    power = jnp.einsum(
        "cij,cjk->cik",
        stat_next,
        bases,
        precision=lax.Precision.HIGHEST,
        preferred_element_type=jnp.float32,
    )
    iterate = power / (
        2.0 * jnp.sqrt(full_cols * jnp.mean(power * power, axis=(1, 2), keepdims=True) + 1e-06)
    )
    iterate = refine(iterate)

    my_slots = myself * capacity + jnp.arange(capacity, dtype=jnp.int32)
    filled = jnp.any(my_slots[:, None] == slot_id[None, :], axis=1)[:, None, None]
    new_stats = jnp.where(filled, stat_next, 0.0)
    new_bases = jnp.where(filled, iterate, 0.0)
    new_second = jnp.where(filled, second_next, 0.0).astype(jnp.bfloat16)
    return (new_moments, update, new_stats, new_bases, new_second)


def solution(mesh):
    placed = (
        P(None, "owner", "tensor"),
        P(None, "owner", "tensor"),
        P(("owner", "tensor"), None, None),
        P(("owner", "tensor"), None, None),
        P(("owner", "tensor"), None, None),
        P(),
    )
    return jax.shard_map(
        local,
        mesh=mesh,
        in_specs=placed,
        out_specs=(
            P(None, "owner", "tensor"),
            P(None, "owner", "tensor"),
            P(("owner", "tensor"), None, None),
            P(("owner", "tensor"), None, None),
            P(("owner", "tensor"), None, None),
        ),
        check_vma=False,
    )
```

```python
import jax
import jax.numpy as jnp
from jax import lax
from jax.sharding import PartitionSpec as P


def refine(iterate):
    for sweep in range(2):
        iter_b = iterate.astype(jnp.bfloat16)
        square = jnp.einsum(
            "cki,ckj->cij", iter_b, iter_b, preferred_element_type=jnp.float32
        ).astype(jnp.bfloat16)
        iterate = 1.5 * iterate - 0.5 * jnp.einsum(
            "cik,ckj->cij", iter_b, square, preferred_element_type=jnp.float32
        )
    return iterate


def exchange(pieces):
    return lax.all_to_all(
        pieces, ("tensor", "owner"), split_axis=0, concat_axis=0, tiled=True
    )


def local(gradients, moments, stats, bases, second, owner_list):
    matrices, piece_rows, piece_cols = gradients.shape
    capacity = stats.shape[0]
    owners = lax.axis_size("owner")
    tensors = lax.axis_size("tensor")
    devices = owners * tensors
    myself = lax.axis_index(("owner", "tensor"))
    matrix_ids = jnp.arange(matrices, dtype=jnp.int32)
    shared = owner_list[:, None] == owner_list[None, :]
    earlier = matrix_ids[:, None] < matrix_ids[None, :]
    position = jnp.sum((shared & earlier).astype(jnp.int32), axis=0)
    slot_id = owner_list * capacity + position
    place = jnp.arange(devices, dtype=jnp.int32)
    device_at = (place % owners) * tensors + place // owners
    targets = device_at[:, None] * capacity + jnp.arange(capacity, dtype=jnp.int32)[None, :]
    hit = targets[:, :, None] == slot_id[None, None, :]
    which = jnp.sum(jnp.where(hit, matrix_ids[None, None, :], 0), axis=2)

    got_grads = exchange(jnp.take(gradients, which, axis=0, mode="clip"))
    new_moments = (0.9 * moments.astype(jnp.float32) + 0.1 * gradients.astype(jnp.float32)).astype(
        jnp.bfloat16
    )
    got_moms = exchange(jnp.take(new_moments, which, axis=0, mode="clip"))

    def column_blocks(pieces):
        return pieces.reshape(tensors, owners * piece_rows, piece_cols)

    full_rows = owners * piece_rows
    full_cols = tensors * piece_cols
    basis_b = bases.astype(jnp.bfloat16)
    stat_list, second_list = [], []
    for c in range(capacity):
        grad_b = column_blocks(got_grads[:, c])
        basis_rows = basis_b[c].reshape(tensors, piece_cols, full_cols)
        gram = jnp.einsum(
            "tik,sil->tksl", grad_b, grad_b, preferred_element_type=jnp.float32
        ).reshape(full_cols, full_cols)
        stat_list.append(0.95 * stats[c] + 0.05 / full_rows * gram)
        rotated = jnp.einsum(
            "tik,tkj->ij", grad_b, basis_rows, preferred_element_type=jnp.float32
        )
        second_list.append(0.95 * second[c].astype(jnp.float32) + 0.05 * rotated * rotated)
    stat_next = jnp.stack(stat_list)
    power = jnp.einsum(
        "cij,cjk->cik",
        stat_next,
        bases,
        precision=lax.Precision.HIGHEST,
        preferred_element_type=jnp.float32,
    )
    iterate = power / (
        2.0 * jnp.sqrt(full_cols * jnp.mean(power * power, axis=(1, 2), keepdims=True) + 1e-06)
    )
    iterate = refine(iterate)
    got_moms, second_list, stat_next, iterate = lax.optimization_barrier(
        (got_moms, second_list, stat_next, iterate)
    )
    steps = []
    for c in range(capacity):
        basis_rows = basis_b[c].reshape(tensors, piece_cols, full_cols)
        moment_rot = jnp.einsum(
            "tik,tkj->ij", column_blocks(got_moms[:, c]), basis_rows,
            preferred_element_type=jnp.float32,
        )
        scaled = (moment_rot / (jnp.sqrt(second_list[c]) + 1e-06)).astype(jnp.bfloat16)
        scaled = lax.optimization_barrier(scaled)
        step_b = jnp.einsum(
            "ij,tkj->tik", scaled, basis_rows, preferred_element_type=jnp.float32
        ).astype(jnp.bfloat16)
        steps.append(step_b.reshape(devices, piece_rows, piece_cols))
    returned = exchange(jnp.stack(steps, axis=1))
    owner_place = (owner_list % tensors) * owners + owner_list // tensors
    update = jnp.take(
        returned.reshape(devices * capacity, piece_rows, piece_cols),
        owner_place * capacity + position, axis=0, mode="clip",
    )

    second_next = jnp.stack(second_list)

    my_slots = myself * capacity + jnp.arange(capacity, dtype=jnp.int32)
    filled = jnp.any(my_slots[:, None] == slot_id[None, :], axis=1)[:, None, None]
    new_stats = jnp.where(filled, stat_next, 0.0)
    new_bases = jnp.where(filled, iterate, 0.0)
    new_second = jnp.where(filled, second_next, 0.0).astype(jnp.bfloat16)
    return (new_moments, update, new_stats, new_bases, new_second)


def solution(mesh):
    placed = (
        P(None, "owner", "tensor"),
        P(None, "owner", "tensor"),
        P(("owner", "tensor"), None, None),
        P(("owner", "tensor"), None, None),
        P(("owner", "tensor"), None, None),
        P(),
    )
    return jax.shard_map(
        local,
        mesh=mesh,
        in_specs=placed,
        out_specs=(
            P(None, "owner", "tensor"),
            P(None, "owner", "tensor"),
            P(("owner", "tensor"), None, None),
            P(("owner", "tensor"), None, None),
            P(("owner", "tensor"), None, None),
        ),
        check_vma=False,
    )
```

```python
import jax
import jax.numpy as jnp
from jax import lax
from jax.sharding import PartitionSpec as P


def refine(iterate):
    for sweep in range(2):
        iter_b = iterate.astype(jnp.bfloat16)
        square = jnp.einsum(
            "cki,ckj->cij", iter_b, iter_b, preferred_element_type=jnp.float32
        ).astype(jnp.bfloat16)
        iterate = 1.5 * iterate - 0.5 * jnp.einsum(
            "cik,ckj->cij", iter_b, square, preferred_element_type=jnp.float32
        )
    return iterate


def exchange(pieces):
    return lax.all_to_all(
        pieces, ("tensor", "owner"), split_axis=0, concat_axis=0, tiled=True
    )


def local(gradients, moments, stats, bases, second, owner_list):
    matrices, piece_rows, piece_cols = gradients.shape
    capacity = stats.shape[0]
    owners = lax.axis_size("owner")
    tensors = lax.axis_size("tensor")
    devices = owners * tensors
    myself = lax.axis_index(("owner", "tensor"))
    matrix_ids = jnp.arange(matrices, dtype=jnp.int32)
    shared = owner_list[:, None] == owner_list[None, :]
    earlier = matrix_ids[:, None] < matrix_ids[None, :]
    position = jnp.sum((shared & earlier).astype(jnp.int32), axis=0)
    slot_id = owner_list * capacity + position
    place = jnp.arange(devices, dtype=jnp.int32)
    device_at = (place % owners) * tensors + place // owners
    targets = device_at[:, None] * capacity + jnp.arange(capacity, dtype=jnp.int32)[None, :]
    hit = targets[:, :, None] == slot_id[None, None, :]
    which = jnp.sum(jnp.where(hit, matrix_ids[None, None, :], 0), axis=2)

    got_grads = exchange(jnp.take(gradients, which, axis=0, mode="clip"))
    new_moments = (0.9 * moments.astype(jnp.float32) + 0.1 * gradients.astype(jnp.float32)).astype(
        jnp.bfloat16
    )
    got_moms = exchange(jnp.take(new_moments, which, axis=0, mode="clip"))

    def column_blocks(pieces):
        return pieces.reshape(tensors, owners * piece_rows, piece_cols)

    full_rows = owners * piece_rows
    full_cols = tensors * piece_cols
    basis_b = bases.astype(jnp.bfloat16)
    stat_list, second_list = [], []
    for c in range(capacity):
        grad_b = column_blocks(got_grads[:, c])
        basis_rows = basis_b[c].reshape(tensors, piece_cols, full_cols)
        gram = jnp.einsum(
            "tik,sil->tksl", grad_b, grad_b, preferred_element_type=jnp.float32
        ).reshape(full_cols, full_cols)
        stat_list.append(0.95 * stats[c] + 0.05 / full_rows * gram)
        rotated = jnp.einsum(
            "tik,tkj->ij", grad_b, basis_rows, preferred_element_type=jnp.float32
        )
        second_list.append(0.95 * second[c].astype(jnp.float32) + 0.05 * rotated * rotated)
    stat_next = jnp.stack(stat_list)
    power = jnp.einsum(
        "cij,cjk->cik",
        stat_next,
        bases,
        precision=lax.Precision.HIGHEST,
        preferred_element_type=jnp.float32,
    )
    got_moms, second_list, power = lax.optimization_barrier((got_moms, second_list, power))
    steps = []
    for c in range(capacity):
        basis_rows = basis_b[c].reshape(tensors, piece_cols, full_cols)
        moment_rot = jnp.einsum(
            "tik,tkj->ij", column_blocks(got_moms[:, c]), basis_rows,
            preferred_element_type=jnp.float32,
        )
        scaled = (moment_rot / (jnp.sqrt(second_list[c]) + 1e-06)).astype(jnp.bfloat16)
        scaled = lax.optimization_barrier(scaled)
        step_b = jnp.einsum(
            "ij,tkj->tik", scaled, basis_rows, preferred_element_type=jnp.float32
        ).astype(jnp.bfloat16)
        steps.append(step_b.reshape(devices, piece_rows, piece_cols))
    returned = exchange(jnp.stack(steps, axis=1))
    owner_place = (owner_list % tensors) * owners + owner_list // tensors
    update = jnp.take(
        returned.reshape(devices * capacity, piece_rows, piece_cols),
        owner_place * capacity + position, axis=0, mode="clip",
    )

    second_next = jnp.stack(second_list)
    iterate = power / (
        2.0 * jnp.sqrt(full_cols * jnp.mean(power * power, axis=(1, 2), keepdims=True) + 1e-06)
    )
    iterate = refine(iterate)

    my_slots = myself * capacity + jnp.arange(capacity, dtype=jnp.int32)
    filled = jnp.any(my_slots[:, None] == slot_id[None, :], axis=1)[:, None, None]
    new_stats = jnp.where(filled, stat_next, 0.0)
    new_bases = jnp.where(filled, iterate, 0.0)
    new_second = jnp.where(filled, second_next, 0.0).astype(jnp.bfloat16)
    return (new_moments, update, new_stats, new_bases, new_second)


def solution(mesh):
    placed = (
        P(None, "owner", "tensor"),
        P(None, "owner", "tensor"),
        P(("owner", "tensor"), None, None),
        P(("owner", "tensor"), None, None),
        P(("owner", "tensor"), None, None),
        P(),
    )
    return jax.shard_map(
        local,
        mesh=mesh,
        in_specs=placed,
        out_specs=(
            P(None, "owner", "tensor"),
            P(None, "owner", "tensor"),
            P(("owner", "tensor"), None, None),
            P(("owner", "tensor"), None, None),
            P(("owner", "tensor"), None, None),
        ),
        check_vma=False,
    )
```

```python
import jax
import jax.numpy as jnp
from jax import lax
from jax.sharding import PartitionSpec as P


def refine(iterate):
    for sweep in range(2):
        iter_b = iterate.astype(jnp.bfloat16)
        square = jnp.einsum(
            "cki,ckj->cij", iter_b, iter_b, preferred_element_type=jnp.float32
        ).astype(jnp.bfloat16)
        iterate = 1.5 * iterate - 0.5 * jnp.einsum(
            "cik,ckj->cij", iter_b, square, preferred_element_type=jnp.float32
        )
    return iterate


def exchange(pieces):
    return lax.all_to_all(
        pieces, ("tensor", "owner"), split_axis=0, concat_axis=0, tiled=True
    )


def local(gradients, moments, stats, bases, second, owner_list):
    matrices, piece_rows, piece_cols = gradients.shape
    capacity = stats.shape[0]
    owners = lax.axis_size("owner")
    tensors = lax.axis_size("tensor")
    devices = owners * tensors
    myself = lax.axis_index(("owner", "tensor"))
    matrix_ids = jnp.arange(matrices, dtype=jnp.int32)
    shared = owner_list[:, None] == owner_list[None, :]
    earlier = matrix_ids[:, None] < matrix_ids[None, :]
    position = jnp.sum((shared & earlier).astype(jnp.int32), axis=0)
    slot_id = owner_list * capacity + position
    place = jnp.arange(devices, dtype=jnp.int32)
    device_at = (place % owners) * tensors + place // owners
    targets = device_at[:, None] * capacity + jnp.arange(capacity, dtype=jnp.int32)[None, :]
    hit = targets[:, :, None] == slot_id[None, None, :]
    pick = hit.astype(jnp.bfloat16)

    def pack(pieces):
        return jnp.einsum(
            "dcn,nrk->dcrk", pick, pieces, preferred_element_type=jnp.float32
        ).astype(jnp.bfloat16)

    got_grads = exchange(pack(gradients))
    new_moments = (0.9 * moments.astype(jnp.float32) + 0.1 * gradients.astype(jnp.float32)).astype(
        jnp.bfloat16
    )
    got_moms = exchange(pack(new_moments))

    def column_blocks(pieces):
        return pieces.reshape(tensors, owners * piece_rows, piece_cols)

    full_rows = owners * piece_rows
    full_cols = tensors * piece_cols
    basis_b = bases.astype(jnp.bfloat16)
    stat_list, second_list = [], []
    for c in range(capacity):
        grad_b = column_blocks(got_grads[:, c])
        basis_rows = basis_b[c].reshape(tensors, piece_cols, full_cols)
        gram = jnp.einsum(
            "tik,sil->tksl", grad_b, grad_b, preferred_element_type=jnp.float32
        ).reshape(full_cols, full_cols)
        stat_list.append(0.95 * stats[c] + 0.05 / full_rows * gram)
        rotated = jnp.einsum(
            "tik,tkj->ij", grad_b, basis_rows, preferred_element_type=jnp.float32
        )
        second_list.append(0.95 * second[c].astype(jnp.float32) + 0.05 * rotated * rotated)
    got_moms, second_list = lax.optimization_barrier((got_moms, second_list))
    steps = []
    for c in range(capacity):
        basis_rows = basis_b[c].reshape(tensors, piece_cols, full_cols)
        moment_rot = jnp.einsum(
            "tik,tkj->ij", column_blocks(got_moms[:, c]), basis_rows,
            preferred_element_type=jnp.float32,
        )
        scaled = (moment_rot / (jnp.sqrt(second_list[c]) + 1e-06)).astype(jnp.bfloat16)
        scaled = lax.optimization_barrier(scaled)
        step_b = jnp.einsum(
            "ij,tkj->tik", scaled, basis_rows, preferred_element_type=jnp.float32
        ).astype(jnp.bfloat16)
        steps.append(step_b.reshape(devices, piece_rows, piece_cols))
    returned = exchange(jnp.stack(steps, axis=1))
    update = jnp.einsum(
        "dcn,dcrk->nrk", pick, returned, preferred_element_type=jnp.float32
    ).astype(jnp.bfloat16)

    stat_next = jnp.stack(stat_list)
    second_next = jnp.stack(second_list)
    power = jnp.einsum(
        "cij,cjk->cik",
        stat_next,
        bases,
        precision=lax.Precision.HIGHEST,
        preferred_element_type=jnp.float32,
    )
    iterate = power / (
        2.0 * jnp.sqrt(full_cols * jnp.mean(power * power, axis=(1, 2), keepdims=True) + 1e-06)
    )
    iterate = refine(iterate)

    my_slots = myself * capacity + jnp.arange(capacity, dtype=jnp.int32)
    filled = jnp.any(my_slots[:, None] == slot_id[None, :], axis=1)[:, None, None]
    new_stats = jnp.where(filled, stat_next, 0.0)
    new_bases = jnp.where(filled, iterate, 0.0)
    new_second = jnp.where(filled, second_next, 0.0).astype(jnp.bfloat16)
    return (new_moments, update, new_stats, new_bases, new_second)


def solution(mesh):
    placed = (
        P(None, "owner", "tensor"),
        P(None, "owner", "tensor"),
        P(("owner", "tensor"), None, None),
        P(("owner", "tensor"), None, None),
        P(("owner", "tensor"), None, None),
        P(),
    )
    return jax.shard_map(
        local,
        mesh=mesh,
        in_specs=placed,
        out_specs=(
            P(None, "owner", "tensor"),
            P(None, "owner", "tensor"),
            P(("owner", "tensor"), None, None),
            P(("owner", "tensor"), None, None),
            P(("owner", "tensor"), None, None),
        ),
        check_vma=False,
    )
```

```python
import jax
import jax.numpy as jnp
from jax import lax
from jax.experimental import pallas as pl
from jax.experimental.pallas import tpu as pltpu
from jax.sharding import PartitionSpec as P


def refine(iterate):
    for sweep in range(2):
        iter_b = iterate.astype(jnp.bfloat16)
        square = jnp.einsum(
            "cki,ckj->cij", iter_b, iter_b, preferred_element_type=jnp.float32
        ).astype(jnp.bfloat16)
        iterate = 1.5 * iterate - 0.5 * jnp.einsum(
            "cik,ckj->cij", iter_b, square, preferred_element_type=jnp.float32
        )
    return iterate


def _gather_kernel(index_ref, source_ref, out_ref, sems):
    count = out_ref.shape[0]

    def start(i, carry):
        pltpu.make_async_copy(source_ref.at[index_ref[i]], out_ref.at[i], sems.at[i]).start()
        return carry

    def wait(i, carry):
        pltpu.make_async_copy(source_ref.at[0], out_ref.at[i], sems.at[i]).wait()
        return carry

    lax.fori_loop(0, count, start, 0)
    lax.fori_loop(0, count, wait, 0)


def gather_rows(source, index):
    count = index.shape[0]
    index = jnp.clip(index, 0, source.shape[0] - 1).astype(jnp.int32)
    row_bytes = source.size // source.shape[0] * source.dtype.itemsize
    return pl.pallas_call(
        _gather_kernel,
        out_shape=jax.ShapeDtypeStruct((count,) + source.shape[1:], source.dtype),
        grid_spec=pltpu.PrefetchScalarGridSpec(
            num_scalar_prefetch=1,
            grid=(1,),
            in_specs=[pl.BlockSpec(memory_space=pl.ANY)],
            out_specs=pl.BlockSpec(memory_space=pl.ANY),
            scratch_shapes=[pltpu.SemaphoreType.DMA((count,))],
        ),
        cost_estimate=pl.CostEstimate(
            flops=0, transcendentals=0, bytes_accessed=2 * count * row_bytes
        ),
    )(index, source)


def exchange(pieces):
    return lax.all_to_all(
        pieces, ("tensor", "owner"), split_axis=0, concat_axis=0, tiled=True
    )


def local(gradients, moments, stats, bases, second, owner_list):
    matrices, piece_rows, piece_cols = gradients.shape
    capacity = stats.shape[0]
    owners = lax.axis_size("owner")
    tensors = lax.axis_size("tensor")
    devices = owners * tensors
    myself = lax.axis_index(("owner", "tensor"))
    matrix_ids = jnp.arange(matrices, dtype=jnp.int32)
    shared = owner_list[:, None] == owner_list[None, :]
    earlier = matrix_ids[:, None] < matrix_ids[None, :]
    position = jnp.sum((shared & earlier).astype(jnp.int32), axis=0)
    slot_id = owner_list * capacity + position
    place = jnp.arange(devices, dtype=jnp.int32)
    device_at = (place % owners) * tensors + place // owners
    targets = device_at[:, None] * capacity + jnp.arange(capacity, dtype=jnp.int32)[None, :]
    hit = targets[:, :, None] == slot_id[None, None, :]
    which = jnp.sum(jnp.where(hit, matrix_ids[None, None, :], 0), axis=2)

    got_grads = exchange(
        gather_rows(gradients, which.reshape(-1)).reshape(devices, capacity, piece_rows, piece_cols)
    )
    new_moments = (0.9 * moments.astype(jnp.float32) + 0.1 * gradients.astype(jnp.float32)).astype(
        jnp.bfloat16
    )
    got_moms = exchange(
        gather_rows(new_moments, which.reshape(-1)).reshape(devices, capacity, piece_rows, piece_cols)
    )

    def column_blocks(pieces):
        return pieces.reshape(tensors, owners * piece_rows, piece_cols)

    full_rows = owners * piece_rows
    full_cols = tensors * piece_cols
    basis_b = bases.astype(jnp.bfloat16)
    stat_list, second_list = [], []
    for c in range(capacity):
        grad_b = column_blocks(got_grads[:, c])
        basis_rows = basis_b[c].reshape(tensors, piece_cols, full_cols)
        gram = jnp.einsum(
            "tik,sil->tksl", grad_b, grad_b, preferred_element_type=jnp.float32
        ).reshape(full_cols, full_cols)
        stat_list.append(0.95 * stats[c] + 0.05 / full_rows * gram)
        rotated = jnp.einsum(
            "tik,tkj->ij", grad_b, basis_rows, preferred_element_type=jnp.float32
        )
        second_list.append(0.95 * second[c].astype(jnp.float32) + 0.05 * rotated * rotated)
    got_moms, second_list = lax.optimization_barrier((got_moms, second_list))
    steps = []
    for c in range(capacity):
        basis_rows = basis_b[c].reshape(tensors, piece_cols, full_cols)
        moment_rot = jnp.einsum(
            "tik,tkj->ij", column_blocks(got_moms[:, c]), basis_rows,
            preferred_element_type=jnp.float32,
        )
        scaled = (moment_rot / (jnp.sqrt(second_list[c]) + 1e-06)).astype(jnp.bfloat16)
        scaled = lax.optimization_barrier(scaled)
        step_b = jnp.einsum(
            "ij,tkj->tik", scaled, basis_rows, preferred_element_type=jnp.float32
        ).astype(jnp.bfloat16)
        steps.append(step_b.reshape(devices, piece_rows, piece_cols))
    returned = exchange(jnp.stack(steps, axis=1))
    owner_place = (owner_list % tensors) * owners + owner_list // tensors
    update = gather_rows(
        returned.reshape(devices * capacity, piece_rows, piece_cols), owner_place * capacity + position
    )

    stat_next = jnp.stack(stat_list)
    second_next = jnp.stack(second_list)
    power = jnp.einsum(
        "cij,cjk->cik",
        stat_next,
        bases,
        precision=lax.Precision.HIGHEST,
        preferred_element_type=jnp.float32,
    )
    iterate = power / (
        2.0 * jnp.sqrt(full_cols * jnp.mean(power * power, axis=(1, 2), keepdims=True) + 1e-06)
    )
    iterate = refine(iterate)

    my_slots = myself * capacity + jnp.arange(capacity, dtype=jnp.int32)
    filled = jnp.any(my_slots[:, None] == slot_id[None, :], axis=1)[:, None, None]
    new_stats = jnp.where(filled, stat_next, 0.0)
    new_bases = jnp.where(filled, iterate, 0.0)
    new_second = jnp.where(filled, second_next, 0.0).astype(jnp.bfloat16)
    return (new_moments, update, new_stats, new_bases, new_second)


def solution(mesh):
    placed = (
        P(None, "owner", "tensor"),
        P(None, "owner", "tensor"),
        P(("owner", "tensor"), None, None),
        P(("owner", "tensor"), None, None),
        P(("owner", "tensor"), None, None),
        P(),
    )
    return jax.shard_map(
        local,
        mesh=mesh,
        in_specs=placed,
        out_specs=(
            P(None, "owner", "tensor"),
            P(None, "owner", "tensor"),
            P(("owner", "tensor"), None, None),
            P(("owner", "tensor"), None, None),
            P(("owner", "tensor"), None, None),
        ),
        check_vma=False,
    )
```

```python
import jax
import jax.numpy as jnp
from jax import lax
from jax.sharding import PartitionSpec as P


def refine(iterate):
    for sweep in range(2):
        iter_b = iterate.astype(jnp.bfloat16)
        square = jnp.einsum(
            "cki,ckj->cij", iter_b, iter_b, preferred_element_type=jnp.float32
        ).astype(jnp.bfloat16)
        iterate = 1.5 * iterate - 0.5 * jnp.einsum(
            "cik,ckj->cij", iter_b, square, preferred_element_type=jnp.float32
        )
    return iterate


def exchange(pieces):
    return lax.all_to_all(
        pieces, ("tensor", "owner"), split_axis=0, concat_axis=0, tiled=True
    )


def local(gradients, moments, stats, bases, second, owner_list):
    matrices, piece_rows, piece_cols = gradients.shape
    capacity = stats.shape[0]
    owners = lax.axis_size("owner")
    tensors = lax.axis_size("tensor")
    devices = owners * tensors
    myself = lax.axis_index(("owner", "tensor"))
    matrix_ids = jnp.arange(matrices, dtype=jnp.int32)
    shared = owner_list[:, None] == owner_list[None, :]
    earlier = matrix_ids[:, None] < matrix_ids[None, :]
    position = jnp.sum((shared & earlier).astype(jnp.int32), axis=0)
    slot_id = owner_list * capacity + position
    place = jnp.arange(devices, dtype=jnp.int32)
    device_at = (place % owners) * tensors + place // owners
    targets = device_at[:, None] * capacity + jnp.arange(capacity, dtype=jnp.int32)[None, :]
    hit = targets[:, :, None] == slot_id[None, None, :]
    which = jnp.sum(jnp.where(hit, matrix_ids[None, None, :], 0), axis=2)

    got_grads = exchange(jnp.take(gradients, which, axis=0, mode="clip"))
    new_moments = (0.9 * moments.astype(jnp.float32) + 0.1 * gradients.astype(jnp.float32)).astype(
        jnp.bfloat16
    )
    got_moms = exchange(jnp.take(new_moments, which, axis=0, mode="clip"))

    def column_blocks(pieces):
        return pieces.reshape(tensors, owners * piece_rows, piece_cols)

    full_rows = owners * piece_rows
    full_cols = tensors * piece_cols
    basis_b = bases.astype(jnp.bfloat16)
    stat_list, second_list = [], []
    for c in range(capacity):
        grad_b = column_blocks(got_grads[:, c])
        basis_rows = basis_b[c].reshape(tensors, piece_cols, full_cols)
        gram = jnp.einsum(
            "tik,sil->tksl", grad_b, grad_b, preferred_element_type=jnp.float32
        ).reshape(full_cols, full_cols)
        stat_list.append(0.95 * stats[c] + 0.05 / full_rows * gram)
        rotated = jnp.einsum(
            "tik,tkj->ij", grad_b, basis_rows, preferred_element_type=jnp.float32
        )
        second_list.append(
            (0.95 * second[c].astype(jnp.float32) + 0.05 * rotated * rotated).astype(jnp.bfloat16)
        )
    got_moms, second_list = lax.optimization_barrier((got_moms, second_list))
    steps = []
    for c in range(capacity):
        basis_rows = basis_b[c].reshape(tensors, piece_cols, full_cols)
        moment_rot = jnp.einsum(
            "tik,tkj->ij", column_blocks(got_moms[:, c]), basis_rows,
            preferred_element_type=jnp.float32,
        )
        scaled = (moment_rot / (jnp.sqrt(second_list[c].astype(jnp.float32)) + 1e-06)).astype(jnp.bfloat16)
        scaled = lax.optimization_barrier(scaled)
        step_b = jnp.einsum(
            "ij,tkj->tik", scaled, basis_rows, preferred_element_type=jnp.float32
        ).astype(jnp.bfloat16)
        steps.append(step_b.reshape(devices, piece_rows, piece_cols))
    returned = exchange(jnp.stack(steps, axis=1))
    owner_place = (owner_list % tensors) * owners + owner_list // tensors
    update = jnp.take(
        returned.reshape(devices * capacity, piece_rows, piece_cols),
        owner_place * capacity + position, axis=0, mode="clip",
    )

    stat_next = jnp.stack(stat_list)
    second_next = jnp.stack(second_list)
    power = jnp.einsum(
        "cij,cjk->cik",
        stat_next,
        bases,
        precision=lax.Precision.HIGHEST,
        preferred_element_type=jnp.float32,
    )
    iterate = power / (
        2.0 * jnp.sqrt(full_cols * jnp.mean(power * power, axis=(1, 2), keepdims=True) + 1e-06)
    )
    iterate = refine(iterate)

    my_slots = myself * capacity + jnp.arange(capacity, dtype=jnp.int32)
    filled = jnp.any(my_slots[:, None] == slot_id[None, :], axis=1)[:, None, None]
    new_stats = jnp.where(filled, stat_next, 0.0)
    new_bases = jnp.where(filled, iterate, 0.0)
    new_second = jnp.where(filled, second_next, jnp.zeros_like(second_next))
    return (new_moments, update, new_stats, new_bases, new_second)


def solution(mesh):
    placed = (
        P(None, "owner", "tensor"),
        P(None, "owner", "tensor"),
        P(("owner", "tensor"), None, None),
        P(("owner", "tensor"), None, None),
        P(("owner", "tensor"), None, None),
        P(),
    )
    return jax.shard_map(
        local,
        mesh=mesh,
        in_specs=placed,
        out_specs=(
            P(None, "owner", "tensor"),
            P(None, "owner", "tensor"),
            P(("owner", "tensor"), None, None),
            P(("owner", "tensor"), None, None),
            P(("owner", "tensor"), None, None),
        ),
        check_vma=False,
    )
```

```python
import jax
import jax.numpy as jnp
from jax import lax
from jax.experimental import pallas as pl
from jax.sharding import PartitionSpec as P


def refine(iterate):
    for sweep in range(2):
        iter_b = iterate.astype(jnp.bfloat16)
        square = jnp.einsum(
            "cki,ckj->cij", iter_b, iter_b, preferred_element_type=jnp.float32
        ).astype(jnp.bfloat16)
        iterate = 1.5 * iterate - 0.5 * jnp.einsum(
            "cik,ckj->cij", iter_b, square, preferred_element_type=jnp.float32
        )
    return iterate


def _update_kernel(moms_ref, second_ref, basis_ref, out_ref):
    tensors, owners, piece_rows, piece_cols = moms_ref.shape
    full_rows = owners * piece_rows
    basis = basis_ref[...]
    moment_rot = None
    for t in range(tensors):
        block = moms_ref[t].reshape(full_rows, piece_cols)
        part = jnp.dot(block, basis[t * piece_cols:(t + 1) * piece_cols, :],
                       preferred_element_type=jnp.float32)
        moment_rot = part if moment_rot is None else moment_rot + part
    scaled = (moment_rot / (jnp.sqrt(second_ref[...]) + 1e-06)).astype(jnp.bfloat16)
    for t in range(tensors):
        step = lax.dot_general(scaled, basis[t * piece_cols:(t + 1) * piece_cols, :],
                               (((1,), (1,)), ((), ())), preferred_element_type=jnp.float32)
        out_ref[t] = step.astype(out_ref.dtype).reshape(owners, piece_rows, piece_cols)

def update_pieces(moms, second_next, basis_b):
    tensors, owners, capacity, piece_rows, piece_cols = moms.shape
    full_rows, full_cols = second_next.shape[1:]
    block = pl.BlockSpec((tensors, owners, None, piece_rows, piece_cols), lambda c: (0, 0, c, 0, 0))
    return pl.pallas_call(
        _update_kernel,
        out_shape=jax.ShapeDtypeStruct(moms.shape, jnp.bfloat16),
        grid=(capacity,),
        in_specs=[block,
                  pl.BlockSpec((None, full_rows, full_cols), lambda c: (c, 0, 0)),
                  pl.BlockSpec((None, full_cols, full_cols), lambda c: (c, 0, 0))],
        out_specs=block,
        cost_estimate=pl.CostEstimate(flops=4 * capacity * full_rows * full_cols * full_cols,
            transcendentals=capacity * full_rows * full_cols,
            bytes_accessed=capacity * (4 * full_rows * full_cols + 4 * full_rows * full_cols + 2 * full_cols * full_cols)),
    )(moms, second_next, basis_b)


def exchange(pieces):
    return lax.all_to_all(
        pieces, ("tensor", "owner"), split_axis=0, concat_axis=0, tiled=True
    )


def local(gradients, moments, stats, bases, second, owner_list):
    matrices, piece_rows, piece_cols = gradients.shape
    capacity = stats.shape[0]
    owners = lax.axis_size("owner")
    tensors = lax.axis_size("tensor")
    devices = owners * tensors
    myself = lax.axis_index(("owner", "tensor"))
    matrix_ids = jnp.arange(matrices, dtype=jnp.int32)
    shared = owner_list[:, None] == owner_list[None, :]
    earlier = matrix_ids[:, None] < matrix_ids[None, :]
    position = jnp.sum((shared & earlier).astype(jnp.int32), axis=0)
    slot_id = owner_list * capacity + position
    place = jnp.arange(devices, dtype=jnp.int32)
    device_at = (place % owners) * tensors + place // owners
    targets = device_at[:, None] * capacity + jnp.arange(capacity, dtype=jnp.int32)[None, :]
    hit = targets[:, :, None] == slot_id[None, None, :]
    which = jnp.sum(jnp.where(hit, matrix_ids[None, None, :], 0), axis=2)

    got_grads = exchange(jnp.take(gradients, which, axis=0, mode="clip"))
    new_moments = (0.9 * moments.astype(jnp.float32) + 0.1 * gradients.astype(jnp.float32)).astype(
        jnp.bfloat16
    )
    got_moms = exchange(jnp.take(new_moments, which, axis=0, mode="clip"))

    def column_blocks(pieces):
        return pieces.reshape(tensors, owners * piece_rows, piece_cols)

    full_rows = owners * piece_rows
    full_cols = tensors * piece_cols
    basis_b = bases.astype(jnp.bfloat16)
    stat_list, second_list = [], []
    for c in range(capacity):
        grad_b = column_blocks(got_grads[:, c])
        basis_rows = basis_b[c].reshape(tensors, piece_cols, full_cols)
        gram = jnp.einsum(
            "tik,sil->tksl", grad_b, grad_b, preferred_element_type=jnp.float32
        ).reshape(full_cols, full_cols)
        stat_list.append(0.95 * stats[c] + 0.05 / full_rows * gram)
        rotated = jnp.einsum(
            "tik,tkj->ij", grad_b, basis_rows, preferred_element_type=jnp.float32
        )
        second_list.append(0.95 * second[c].astype(jnp.float32) + 0.05 * rotated * rotated)
    got_moms, second_next = lax.optimization_barrier((got_moms, jnp.stack(second_list)))
    step_pieces = update_pieces(
        got_moms.reshape(tensors, owners, capacity, piece_rows, piece_cols),
        second_next,
        basis_b,
    )
    returned = exchange(step_pieces.reshape(devices, capacity, piece_rows, piece_cols))
    owner_place = (owner_list % tensors) * owners + owner_list // tensors
    update = jnp.take(
        returned.reshape(devices * capacity, piece_rows, piece_cols),
        owner_place * capacity + position, axis=0, mode="clip",
    )

    stat_next = jnp.stack(stat_list)
    power = jnp.einsum(
        "cij,cjk->cik",
        stat_next,
        bases,
        precision=lax.Precision.HIGHEST,
        preferred_element_type=jnp.float32,
    )
    iterate = power / (
        2.0 * jnp.sqrt(full_cols * jnp.mean(power * power, axis=(1, 2), keepdims=True) + 1e-06)
    )
    iterate = refine(iterate)

    my_slots = myself * capacity + jnp.arange(capacity, dtype=jnp.int32)
    filled = jnp.any(my_slots[:, None] == slot_id[None, :], axis=1)[:, None, None]
    new_stats = jnp.where(filled, stat_next, 0.0)
    new_bases = jnp.where(filled, iterate, 0.0)
    new_second = jnp.where(filled, second_next, 0.0).astype(jnp.bfloat16)
    return (new_moments, update, new_stats, new_bases, new_second)


def solution(mesh):
    placed = (
        P(None, "owner", "tensor"),
        P(None, "owner", "tensor"),
        P(("owner", "tensor"), None, None),
        P(("owner", "tensor"), None, None),
        P(("owner", "tensor"), None, None),
        P(),
    )
    return jax.shard_map(
        local,
        mesh=mesh,
        in_specs=placed,
        out_specs=(
            P(None, "owner", "tensor"),
            P(None, "owner", "tensor"),
            P(("owner", "tensor"), None, None),
            P(("owner", "tensor"), None, None),
            P(("owner", "tensor"), None, None),
        ),
        check_vma=False,
    )
```

```python
import jax
import jax.numpy as jnp
from jax import lax
from jax.experimental import pallas as pl
from jax.experimental.pallas import tpu as pltpu
from jax.sharding import PartitionSpec as P


def refine(iterate):
    for sweep in range(2):
        iter_b = iterate.astype(jnp.bfloat16)
        square = jnp.einsum(
            "cki,ckj->cij", iter_b, iter_b, preferred_element_type=jnp.float32
        ).astype(jnp.bfloat16)
        iterate = 1.5 * iterate - 0.5 * jnp.einsum(
            "cik,ckj->cij", iter_b, square, preferred_element_type=jnp.float32
        )
    return iterate


def _update_kernel(moms_ref, second_ref, basis_ref, basis_t_ref, out_ref, assembled):
    tensors, owners, piece_rows, piece_cols = moms_ref.shape
    full_rows = owners * piece_rows
    for t in range(tensors):
        assembled[:, t * piece_cols:(t + 1) * piece_cols] = moms_ref[t].reshape(full_rows, piece_cols)
    moment_rot = jnp.dot(assembled[...], basis_ref[...], preferred_element_type=jnp.float32)
    scaled = (moment_rot / (jnp.sqrt(second_ref[...]) + 1e-06)).astype(jnp.bfloat16)
    step = jnp.dot(scaled, basis_t_ref[...], preferred_element_type=jnp.float32).astype(out_ref.dtype)
    for t in range(tensors):
        out_ref[t] = step[:, t * piece_cols:(t + 1) * piece_cols].reshape(owners, piece_rows, piece_cols)


def update_pieces(moms, second_next, basis_b, basis_t):
    tensors, owners, capacity, piece_rows, piece_cols = moms.shape
    full_rows, full_cols = second_next.shape[1:]
    block = pl.BlockSpec((tensors, owners, None, piece_rows, piece_cols), lambda c: (0, 0, c, 0, 0))
    return pl.pallas_call(
        _update_kernel,
        out_shape=jax.ShapeDtypeStruct(moms.shape, jnp.bfloat16),
        grid=(capacity,),
        in_specs=[block,
                  pl.BlockSpec((None, full_rows, full_cols), lambda c: (c, 0, 0)),
                  pl.BlockSpec((None, full_cols, full_cols), lambda c: (c, 0, 0)),
                  pl.BlockSpec((None, full_cols, full_cols), lambda c: (c, 0, 0))],
        out_specs=block,
        scratch_shapes=[pltpu.VMEM((full_rows, full_cols), jnp.bfloat16)],
        cost_estimate=pl.CostEstimate(flops=4 * capacity * full_rows * full_cols * full_cols,
            transcendentals=capacity * full_rows * full_cols,
            bytes_accessed=capacity * (4 * full_rows * full_cols + 4 * full_rows * full_cols + 2 * full_cols * full_cols)),
    )(moms, second_next, basis_b, basis_t)


def exchange(pieces):
    return lax.all_to_all(
        pieces, ("tensor", "owner"), split_axis=0, concat_axis=0, tiled=True
    )


def local(gradients, moments, stats, bases, second, owner_list):
    matrices, piece_rows, piece_cols = gradients.shape
    capacity = stats.shape[0]
    owners = lax.axis_size("owner")
    tensors = lax.axis_size("tensor")
    devices = owners * tensors
    myself = lax.axis_index(("owner", "tensor"))
    matrix_ids = jnp.arange(matrices, dtype=jnp.int32)
    shared = owner_list[:, None] == owner_list[None, :]
    earlier = matrix_ids[:, None] < matrix_ids[None, :]
    position = jnp.sum((shared & earlier).astype(jnp.int32), axis=0)
    slot_id = owner_list * capacity + position
    place = jnp.arange(devices, dtype=jnp.int32)
    device_at = (place % owners) * tensors + place // owners
    targets = device_at[:, None] * capacity + jnp.arange(capacity, dtype=jnp.int32)[None, :]
    hit = targets[:, :, None] == slot_id[None, None, :]
    which = jnp.sum(jnp.where(hit, matrix_ids[None, None, :], 0), axis=2)

    got_grads = exchange(jnp.take(gradients, which, axis=0, mode="clip"))
    new_moments = (0.9 * moments.astype(jnp.float32) + 0.1 * gradients.astype(jnp.float32)).astype(
        jnp.bfloat16
    )
    got_moms = exchange(jnp.take(new_moments, which, axis=0, mode="clip"))

    def column_blocks(pieces):
        return pieces.reshape(tensors, owners * piece_rows, piece_cols)

    full_rows = owners * piece_rows
    full_cols = tensors * piece_cols
    basis_b = bases.astype(jnp.bfloat16)
    stat_list, second_list = [], []
    for c in range(capacity):
        grad_b = column_blocks(got_grads[:, c])
        basis_rows = basis_b[c].reshape(tensors, piece_cols, full_cols)
        gram = jnp.einsum(
            "tik,sil->tksl", grad_b, grad_b, preferred_element_type=jnp.float32
        ).reshape(full_cols, full_cols)
        stat_list.append(0.95 * stats[c] + 0.05 / full_rows * gram)
        rotated = jnp.einsum(
            "tik,tkj->ij", grad_b, basis_rows, preferred_element_type=jnp.float32
        )
        second_list.append(0.95 * second[c].astype(jnp.float32) + 0.05 * rotated * rotated)
    basis_t = jnp.swapaxes(basis_b, 1, 2)
    got_moms, second_next, basis_t = lax.optimization_barrier(
        (got_moms, jnp.stack(second_list), basis_t)
    )
    step_pieces = update_pieces(
        got_moms.reshape(tensors, owners, capacity, piece_rows, piece_cols),
        second_next,
        basis_b,
        basis_t,
    )
    returned = exchange(step_pieces.reshape(devices, capacity, piece_rows, piece_cols))
    owner_place = (owner_list % tensors) * owners + owner_list // tensors
    update = jnp.take(
        returned.reshape(devices * capacity, piece_rows, piece_cols),
        owner_place * capacity + position, axis=0, mode="clip",
    )

    stat_next = jnp.stack(stat_list)
    power = jnp.einsum(
        "cij,cjk->cik",
        stat_next,
        bases,
        precision=lax.Precision.HIGHEST,
        preferred_element_type=jnp.float32,
    )
    iterate = power / (
        2.0 * jnp.sqrt(full_cols * jnp.mean(power * power, axis=(1, 2), keepdims=True) + 1e-06)
    )
    iterate = refine(iterate)

    my_slots = myself * capacity + jnp.arange(capacity, dtype=jnp.int32)
    filled = jnp.any(my_slots[:, None] == slot_id[None, :], axis=1)[:, None, None]
    new_stats = jnp.where(filled, stat_next, 0.0)
    new_bases = jnp.where(filled, iterate, 0.0)
    new_second = jnp.where(filled, second_next, 0.0).astype(jnp.bfloat16)
    return (new_moments, update, new_stats, new_bases, new_second)


def solution(mesh):
    placed = (
        P(None, "owner", "tensor"),
        P(None, "owner", "tensor"),
        P(("owner", "tensor"), None, None),
        P(("owner", "tensor"), None, None),
        P(("owner", "tensor"), None, None),
        P(),
    )
    return jax.shard_map(
        local,
        mesh=mesh,
        in_specs=placed,
        out_specs=(
            P(None, "owner", "tensor"),
            P(None, "owner", "tensor"),
            P(("owner", "tensor"), None, None),
            P(("owner", "tensor"), None, None),
            P(("owner", "tensor"), None, None),
        ),
        check_vma=False,
    )
```

```python
import jax
import jax.numpy as jnp
from jax import lax
from jax.experimental import pallas as pl
from jax.experimental.pallas import tpu as pltpu
from jax.sharding import PartitionSpec as P


def refine(iterate):
    for sweep in range(2):
        iter_b = iterate.astype(jnp.bfloat16)
        square = jnp.einsum(
            "cki,ckj->cij", iter_b, iter_b, preferred_element_type=jnp.float32
        ).astype(jnp.bfloat16)
        iterate = 1.5 * iterate - 0.5 * jnp.einsum(
            "cik,ckj->cij", iter_b, square, preferred_element_type=jnp.float32
        )
    return iterate


def _update_kernel(moms_ref, second_ref, basis_ref, basis_t_ref, out_ref, assembled):
    tensors, owners, piece_rows, piece_cols = moms_ref.shape
    full_rows = owners * piece_rows
    for t in range(tensors):
        assembled[:, t * piece_cols:(t + 1) * piece_cols] = moms_ref[t].reshape(full_rows, piece_cols)
    moment_rot = jnp.dot(assembled[...], basis_ref[...], preferred_element_type=jnp.float32)
    scaled = (moment_rot / (jnp.sqrt(second_ref[...]) + 1e-06)).astype(jnp.bfloat16)
    step = jnp.dot(scaled, basis_t_ref[...], preferred_element_type=jnp.float32).astype(out_ref.dtype)
    for t in range(tensors):
        out_ref[t] = step[:, t * piece_cols:(t + 1) * piece_cols].reshape(owners, piece_rows, piece_cols)


def update_pieces(moms, second_next, basis_b, basis_t):
    tensors, owners, capacity, piece_rows, piece_cols = moms.shape
    full_rows, full_cols = second_next.shape[1:]
    block = pl.BlockSpec((tensors, owners, None, piece_rows, piece_cols), lambda c: (0, 0, c, 0, 0))
    return pl.pallas_call(
        _update_kernel,
        out_shape=jax.ShapeDtypeStruct(moms.shape, jnp.bfloat16),
        grid=(capacity,),
        in_specs=[block,
                  pl.BlockSpec((None, full_rows, full_cols), lambda c: (c, 0, 0)),
                  pl.BlockSpec((None, full_cols, full_cols), lambda c: (c, 0, 0)),
                  pl.BlockSpec((None, full_cols, full_cols), lambda c: (c, 0, 0))],
        out_specs=block,
        scratch_shapes=[pltpu.VMEM((full_rows, full_cols), jnp.bfloat16)],
        compiler_params=pltpu.CompilerParams(vmem_limit_bytes=24 * 1024 * 1024),
        cost_estimate=pl.CostEstimate(flops=4 * capacity * full_rows * full_cols * full_cols,
            transcendentals=capacity * full_rows * full_cols,
            bytes_accessed=capacity * (4 * full_rows * full_cols + 4 * full_rows * full_cols + 2 * full_cols * full_cols)),
    )(moms, second_next, basis_b, basis_t)


def exchange(pieces):
    return lax.all_to_all(
        pieces, ("tensor", "owner"), split_axis=0, concat_axis=0, tiled=True
    )


def local(gradients, moments, stats, bases, second, owner_list):
    matrices, piece_rows, piece_cols = gradients.shape
    capacity = stats.shape[0]
    owners = lax.axis_size("owner")
    tensors = lax.axis_size("tensor")
    devices = owners * tensors
    myself = lax.axis_index(("owner", "tensor"))
    matrix_ids = jnp.arange(matrices, dtype=jnp.int32)
    shared = owner_list[:, None] == owner_list[None, :]
    earlier = matrix_ids[:, None] < matrix_ids[None, :]
    position = jnp.sum((shared & earlier).astype(jnp.int32), axis=0)
    slot_id = owner_list * capacity + position
    place = jnp.arange(devices, dtype=jnp.int32)
    device_at = (place % owners) * tensors + place // owners
    targets = device_at[:, None] * capacity + jnp.arange(capacity, dtype=jnp.int32)[None, :]
    hit = targets[:, :, None] == slot_id[None, None, :]
    which = jnp.sum(jnp.where(hit, matrix_ids[None, None, :], 0), axis=2)

    got_grads = exchange(jnp.take(gradients, which, axis=0, mode="clip"))
    new_moments = (0.9 * moments.astype(jnp.float32) + 0.1 * gradients.astype(jnp.float32)).astype(
        jnp.bfloat16
    )
    got_moms = exchange(jnp.take(new_moments, which, axis=0, mode="clip"))

    def column_blocks(pieces):
        return pieces.reshape(tensors, owners * piece_rows, piece_cols)

    full_rows = owners * piece_rows
    full_cols = tensors * piece_cols
    basis_b = bases.astype(jnp.bfloat16)
    stat_list, second_list = [], []
    for c in range(capacity):
        grad_b = column_blocks(got_grads[:, c])
        basis_rows = basis_b[c].reshape(tensors, piece_cols, full_cols)
        gram = jnp.einsum(
            "tik,sil->tksl", grad_b, grad_b, preferred_element_type=jnp.float32
        ).reshape(full_cols, full_cols)
        stat_list.append(0.95 * stats[c] + 0.05 / full_rows * gram)
        rotated = jnp.einsum(
            "tik,tkj->ij", grad_b, basis_rows, preferred_element_type=jnp.float32
        )
        second_list.append(0.95 * second[c].astype(jnp.float32) + 0.05 * rotated * rotated)
    basis_t = jnp.swapaxes(basis_b, 1, 2)
    got_moms, second_next, basis_t = lax.optimization_barrier(
        (got_moms, jnp.stack(second_list), basis_t)
    )
    step_pieces = update_pieces(
        got_moms.reshape(tensors, owners, capacity, piece_rows, piece_cols),
        second_next,
        basis_b,
        basis_t,
    )
    returned = exchange(step_pieces.reshape(devices, capacity, piece_rows, piece_cols))
    owner_place = (owner_list % tensors) * owners + owner_list // tensors
    update = jnp.take(
        returned.reshape(devices * capacity, piece_rows, piece_cols),
        owner_place * capacity + position, axis=0, mode="clip",
    )

    stat_next = jnp.stack(stat_list)
    power = jnp.einsum(
        "cij,cjk->cik",
        stat_next,
        bases,
        precision=lax.Precision.HIGHEST,
        preferred_element_type=jnp.float32,
    )
    iterate = power / (
        2.0 * jnp.sqrt(full_cols * jnp.mean(power * power, axis=(1, 2), keepdims=True) + 1e-06)
    )
    iterate = refine(iterate)

    my_slots = myself * capacity + jnp.arange(capacity, dtype=jnp.int32)
    filled = jnp.any(my_slots[:, None] == slot_id[None, :], axis=1)[:, None, None]
    new_stats = jnp.where(filled, stat_next, 0.0)
    new_bases = jnp.where(filled, iterate, 0.0)
    new_second = jnp.where(filled, second_next, 0.0).astype(jnp.bfloat16)
    return (new_moments, update, new_stats, new_bases, new_second)


def solution(mesh):
    placed = (
        P(None, "owner", "tensor"),
        P(None, "owner", "tensor"),
        P(("owner", "tensor"), None, None),
        P(("owner", "tensor"), None, None),
        P(("owner", "tensor"), None, None),
        P(),
    )
    return jax.shard_map(
        local,
        mesh=mesh,
        in_specs=placed,
        out_specs=(
            P(None, "owner", "tensor"),
            P(None, "owner", "tensor"),
            P(("owner", "tensor"), None, None),
            P(("owner", "tensor"), None, None),
            P(("owner", "tensor"), None, None),
        ),
        check_vma=False,
    )
```

```python
import jax
import jax.numpy as jnp
from jax import lax
from jax.sharding import PartitionSpec as P


def refine(iterate):
    for sweep in range(2):
        iter_b = iterate.astype(jnp.bfloat16)
        square = jnp.einsum(
            "cki,ckj->cij", iter_b, iter_b, preferred_element_type=jnp.float32
        ).astype(jnp.bfloat16)
        iterate = 1.5 * iterate - 0.5 * jnp.einsum(
            "cik,ckj->cij", iter_b, square, preferred_element_type=jnp.float32
        )
    return iterate


def exchange(pieces):
    return lax.all_to_all(
        pieces, ("tensor", "owner"), split_axis=0, concat_axis=0, tiled=True
    )


def local(gradients, moments, stats, bases, second, owner_list):
    matrices, piece_rows, piece_cols = gradients.shape
    capacity = stats.shape[0]
    owners = lax.axis_size("owner")
    tensors = lax.axis_size("tensor")
    devices = owners * tensors
    myself = lax.axis_index(("owner", "tensor"))
    matrix_ids = jnp.arange(matrices, dtype=jnp.int32)
    shared = owner_list[:, None] == owner_list[None, :]
    earlier = matrix_ids[:, None] < matrix_ids[None, :]
    position = jnp.sum((shared & earlier).astype(jnp.int32), axis=0)
    slot_id = owner_list * capacity + position
    place = jnp.arange(devices, dtype=jnp.int32)
    device_at = (place % owners) * tensors + place // owners
    owned = device_at[:, None] == owner_list[None, :]
    which = jnp.stack(
        [
            jnp.min(jnp.where(owned, matrix_ids[None, :], matrices - 1), axis=1),
            jnp.max(jnp.where(owned, matrix_ids[None, :], 0), axis=1),
        ],
        axis=1,
    )

    got_grads = exchange(jnp.take(gradients, which, axis=0, mode="clip"))
    new_moments = (0.9 * moments.astype(jnp.float32) + 0.1 * gradients.astype(jnp.float32)).astype(
        jnp.bfloat16
    )
    got_moms = exchange(jnp.take(new_moments, which, axis=0, mode="clip"))

    def column_blocks(pieces):
        return pieces.reshape(tensors, owners * piece_rows, piece_cols)

    full_rows = owners * piece_rows
    full_cols = tensors * piece_cols
    basis_b = bases.astype(jnp.bfloat16)
    stat_list, second_list = [], []
    for c in range(capacity):
        grad_b = column_blocks(got_grads[:, c])
        basis_rows = basis_b[c].reshape(tensors, piece_cols, full_cols)
        gram = jnp.einsum(
            "tik,sil->tksl", grad_b, grad_b, preferred_element_type=jnp.float32
        ).reshape(full_cols, full_cols)
        stat_list.append(0.95 * stats[c] + 0.05 / full_rows * gram)
        rotated = jnp.einsum(
            "tik,tkj->ij", grad_b, basis_rows, preferred_element_type=jnp.float32
        )
        second_list.append(0.95 * second[c].astype(jnp.float32) + 0.05 * rotated * rotated)
    got_moms, second_list = lax.optimization_barrier((got_moms, second_list))
    steps = []
    for c in range(capacity):
        basis_rows = basis_b[c].reshape(tensors, piece_cols, full_cols)
        moment_rot = jnp.einsum(
            "tik,tkj->ij", column_blocks(got_moms[:, c]), basis_rows,
            preferred_element_type=jnp.float32,
        )
        scaled = (moment_rot / (jnp.sqrt(second_list[c]) + 1e-06)).astype(jnp.bfloat16)
        scaled = lax.optimization_barrier(scaled)
        step_b = jnp.einsum(
            "ij,tkj->tik", scaled, basis_rows, preferred_element_type=jnp.float32
        ).astype(jnp.bfloat16)
        steps.append(step_b.reshape(devices, piece_rows, piece_cols))
    returned = exchange(jnp.stack(steps, axis=1))
    owner_place = (owner_list % tensors) * owners + owner_list // tensors
    update = jnp.take(
        returned.reshape(devices * capacity, piece_rows, piece_cols),
        owner_place * capacity + position, axis=0, mode="clip",
    )

    stat_next = jnp.stack(stat_list)
    second_next = jnp.stack(second_list)
    power = jnp.einsum(
        "cij,cjk->cik",
        stat_next,
        bases,
        precision=lax.Precision.HIGHEST,
        preferred_element_type=jnp.float32,
    )
    iterate = power / (
        2.0 * jnp.sqrt(full_cols * jnp.mean(power * power, axis=(1, 2), keepdims=True) + 1e-06)
    )
    iterate = refine(iterate)

    my_slots = myself * capacity + jnp.arange(capacity, dtype=jnp.int32)
    filled = jnp.any(my_slots[:, None] == slot_id[None, :], axis=1)[:, None, None]
    new_stats = jnp.where(filled, stat_next, 0.0)
    new_bases = jnp.where(filled, iterate, 0.0)
    new_second = jnp.where(filled, second_next, 0.0).astype(jnp.bfloat16)
    return (new_moments, update, new_stats, new_bases, new_second)


def solution(mesh):
    placed = (
        P(None, "owner", "tensor"),
        P(None, "owner", "tensor"),
        P(("owner", "tensor"), None, None),
        P(("owner", "tensor"), None, None),
        P(("owner", "tensor"), None, None),
        P(),
    )
    return jax.shard_map(
        local,
        mesh=mesh,
        in_specs=placed,
        out_specs=(
            P(None, "owner", "tensor"),
            P(None, "owner", "tensor"),
            P(("owner", "tensor"), None, None),
            P(("owner", "tensor"), None, None),
            P(("owner", "tensor"), None, None),
        ),
        check_vma=False,
    )
```
